128 devices in a mesh: dp: 16 (over z_hi, x, core), tensor: 8 (over y, z_lo).
Axes of the slice: x: 4, y: 4, z: 4 (z_hi: 2, z_lo: 2; z = z_hi * 2 + z_lo), core: 2. Of those that a mesh axis runs over, the one named last changes fastest.
Arguments:
- layer_input: bfloat16 [16, 1024, 4096], P('dp', 'tensor'), may hold values from -9 to 9
- norm_gain: bfloat16 [4096], replicated, may hold values from 0.5 to 1.5
- w_query: bfloat16 [4096, 2048], P(None, 'tensor'), may hold values from -0.125 to 0.125
- w_key: bfloat16 [4096, 1024], P(None, 'tensor'), may hold values from -0.125 to 0.125
- value_weight: bfloat16 [4096, 1024], P(None, 'tensor'), may hold values from -0.09375 to 0.09375
- w_out: bfloat16 [2048, 4096], P('tensor'), may hold values from -0.125 to 0.125
- prefix_len: int32 [16], P('dp'), may hold values from 128 to 511
- grad_output: bfloat16 [16, 1024, 4096], P('dp', 'tensor'), may hold values from -6 to 6
Outputs:
- layer_output: bfloat16 [16, 1024, 4096], P('dp', 'tensor')
- grad_input: bfloat16 [16, 1024, 4096], P('dp', 'tensor')
- grad_gain: float32 [4096], replicated
- grad_query: bfloat16 [4096, 2048], P('dp', 'tensor')
- grad_key: bfloat16 [4096, 1024], P('dp', 'tensor')
- grad_value: bfloat16 [4096, 1024], P('dp', 'tensor')
- grad_wout: bfloat16 [2048, 4096], P('tensor', 'dp')
The draws below stay inside these ranges and needn't reach their ends.
Inputs may be any that keep to these rules, and one draw needn't show every extreme that they name: `prefix_len`: the number of leading spectrum positions of each replica's sequence that every position attends to.
All inputs are finite; a program needn't handle non-finite values.
Results may differ from the reference program's by a relative error of at most 0.015.
The reference program's roundings to bfloat16 on the way count: a program that leaves them out, or rounds other values in their place, can miss the bound.
Values may be sent and summed in bfloat16 or wider, within the bound.
No kernel may reach another device: no remote copies, remote signals or barrier semaphores. Data moves between devices by JAX's collectives and lax.ppermute only.
A program may use at most 192 MiB of HBM per device.

```python
import jax
import jax.numpy as jnp
from jax import lax

MODEL_WIDTH = 4096
QUERY_HEADS = 16
KEY_VALUE_HEADS = 8
HEAD_SIZE = 128
SEQ = 1024
N_DP = 16
N_TENSOR = 8


def draw_layer_input(key, part):
    rows_noise = jax.random.truncated_normal(jax.random.fold_in(key, 11), -6.0, 6.0, (N_DP, SEQ, MODEL_WIDTH), jnp.float32)
    return rows_noise.astype(jnp.bfloat16)


def draw_w_query(key, part):
    starting_row_block = jax.random.truncated_normal(jax.random.fold_in(key, 21), -6.0, 6.0, (MODEL_WIDTH, QUERY_HEADS * HEAD_SIZE), jnp.float32) * MODEL_WIDTH ** (-0.5)
    return starting_row_block.astype(jnp.bfloat16)


def draw_w_key(key, part):
    starting_row_block = jax.random.truncated_normal(jax.random.fold_in(key, 31), -6.0, 6.0, (MODEL_WIDTH, KEY_VALUE_HEADS * HEAD_SIZE), jnp.float32) * MODEL_WIDTH ** (-0.5)
    return starting_row_block.astype(jnp.bfloat16)


def touch_ends(array, key, smallest, largest):
    dims = array.shape
    spot = [jax.random.randint(jax.random.fold_in(key, axis), (), 0, dims[axis]) for axis in range(len(dims))]
    array = array.at[tuple(spot)].set(smallest)
    longest = dims.index(max(dims))
    spot[longest] = (spot[longest] + 1) % dims[longest]
    return array.at[tuple(spot)].set(largest)


def shard_levels(own_key, shape, shards, least, largest):
    level, own = 1.0, jax.random.fold_in(own_key, 6)
    for position, parts in shards:
        steps = jnp.exp(jax.random.uniform(jax.random.fold_in(own, position), (parts,), jnp.float32, least / len(shards), largest / len(shards)))
        level = level * jnp.repeat(steps, shape[position] // parts).reshape([-1 if axis == position else 1 for axis in range(len(shape))])
    return level


def gaussian(own_key, dims, scale, most, shards=(), held_as=jnp.bfloat16):
    gain = shard_levels(own_key, dims, shards, -0.22, 0.18) if shards else 1.0
    array = jax.random.normal(own_key, dims, jnp.float32) * scale * gain
    return jnp.minimum(jnp.maximum(array, -most), most).astype(held_as)


def setup_inputs(seed: int = 0) -> dict:
    streams_of = jax.random.split(jax.random.key(seed), 9)
    layer_input = draw_layer_input(jax.random.fold_in(streams_of[8], 71), 0)
    norm_gain = jnp.clip(1.0 + 0.1 * jax.random.normal(streams_of[1], (MODEL_WIDTH,), jnp.float32), 0.5, 1.5).astype(jnp.bfloat16)
    w_query = draw_w_query(jax.random.fold_in(streams_of[8], 71), 0)
    w_key = draw_w_key(jax.random.fold_in(streams_of[8], 71), 0)
    value_weight = gaussian(streams_of[4], (MODEL_WIDTH, KEY_VALUE_HEADS * HEAD_SIZE), MODEL_WIDTH ** -0.5, 0.09375, ((1, 8),))
    w_out = gaussian(streams_of[5], (QUERY_HEADS * HEAD_SIZE, MODEL_WIDTH), (QUERY_HEADS * HEAD_SIZE) ** -0.5, 0.125, ((0, 8),))
    prefix_len = touch_ends(jax.random.randint(streams_of[6], (N_DP,), SEQ // 8, SEQ // 2), jax.random.fold_in(streams_of[6], 1), SEQ // 8, (SEQ // 2) - 1).astype(jnp.int32)
    grad_output = gaussian(streams_of[7], (N_DP, SEQ, MODEL_WIDTH), 1.0, 6.0, ((0, 16), (1, 8)))
    return dict(layer_input=layer_input, norm_gain=norm_gain, w_query=w_query, w_key=w_key, value_weight=value_weight, w_out=w_out, prefix_len=prefix_len, grad_output=grad_output)


EPS = 1e-05

def convert_float(value):
    return value.astype(jnp.float32)

def replica(x_rows, gain_vec, w_query, w_key, value_weight, w_out, prefix, grad_rows):
    sequence_length = x_rows.shape[0]
    heads_per_group = QUERY_HEADS // KEY_VALUE_HEADS
    scale_f = 1.0 / HEAD_SIZE ** 0.5
    rows_f = convert_float(x_rows)
    inv_rms = lax.rsqrt(lax.optimization_barrier(jnp.mean(rows_f * rows_f, axis=1, keepdims=True)) + EPS)
    unit_rows = rows_f * inv_rms
    normed = (unit_rows * gain_vec).astype(jnp.bfloat16)
    query_matrix = jnp.dot(normed, w_query, preferred_element_type=jnp.float32).astype(jnp.bfloat16)
    key_projected = jnp.dot(normed, w_key, preferred_element_type=jnp.float32).astype(jnp.bfloat16)
    value_projected = jnp.dot(normed, value_weight, preferred_element_type=jnp.float32).astype(jnp.bfloat16)
    query_head_rows = convert_float(query_matrix).reshape(sequence_length, KEY_VALUE_HEADS, heads_per_group, HEAD_SIZE)
    key_head_rows = convert_float(key_projected).reshape(sequence_length, KEY_VALUE_HEADS, HEAD_SIZE)
    value_head_rows = convert_float(value_projected).reshape(sequence_length, KEY_VALUE_HEADS, HEAD_SIZE)
    positions = jnp.arange(sequence_length, dtype=jnp.int32)
    allowed = (positions[None, :] <= positions[:, None]) | (positions[None, :] < prefix)
    scores = jnp.einsum('skgd,tkd->kgst', query_head_rows, key_head_rows) * scale_f
    masked = jnp.where(allowed, scores, -1e+30)
    row_max = lax.optimization_barrier(jnp.max(masked, axis=-1, keepdims=True))
    expo_vals = jnp.exp(masked - row_max)
    attn_probs = expo_vals / lax.optimization_barrier(jnp.sum(expo_vals, axis=-1, keepdims=True))
    probability_batch = attn_probs.astype(jnp.bfloat16)
    context = jnp.einsum('kgst,tkd->skgd', convert_float(probability_batch), value_head_rows).astype(jnp.bfloat16).reshape(sequence_length, QUERY_HEADS * HEAD_SIZE)
    group_count = N_TENSOR
    cols_q = QUERY_HEADS * HEAD_SIZE // group_count
    key_value_columns = KEY_VALUE_HEADS * HEAD_SIZE // group_count
    out_terms = jnp.einsum('stc,tcd->tsd', convert_float(context).reshape(sequence_length, group_count, cols_q), convert_float(w_out).reshape(group_count, cols_q, MODEL_WIDTH)).astype(jnp.bfloat16)
    attn_sum = lax.optimization_barrier(jnp.sum(convert_float(out_terms), axis=0))
    layer_output = (rows_f + attn_sum).astype(jnp.bfloat16)
    context_gradient = jnp.dot(grad_rows, w_out.T, preferred_element_type=jnp.float32).astype(jnp.bfloat16)
    grad_wout = jnp.dot(context.T, grad_rows, preferred_element_type=jnp.float32).astype(jnp.bfloat16)
    context_head_gradient = convert_float(context_gradient).reshape(sequence_length, KEY_VALUE_HEADS, heads_per_group, HEAD_SIZE)
    d_probs = jnp.einsum('skgd,tkd->kgst', context_head_gradient, value_head_rows)
    row_delta = lax.optimization_barrier(jnp.sum(d_probs * attn_probs, axis=-1, keepdims=True))
    scores_gradient = convert_float((attn_probs * (d_probs - row_delta) * scale_f).astype(jnp.bfloat16))
    d_query = jnp.einsum('kgst,tkd->skgd', scores_gradient, key_head_rows).astype(jnp.bfloat16).reshape(sequence_length, QUERY_HEADS * HEAD_SIZE)
    key_gradient = jnp.einsum('apyq,yapz->qaz', scores_gradient, query_head_rows).astype(jnp.bfloat16).reshape(sequence_length, KEY_VALUE_HEADS * HEAD_SIZE)
    value_gradient = jnp.einsum('apyq,yapz->qaz', convert_float(probability_batch), context_head_gradient).astype(jnp.bfloat16).reshape(sequence_length, KEY_VALUE_HEADS * HEAD_SIZE)
    grad_wq = jnp.dot(normed.T, d_query, preferred_element_type=jnp.float32).astype(jnp.bfloat16)
    grad_wk = jnp.dot(normed.T, key_gradient, preferred_element_type=jnp.float32).astype(jnp.bfloat16)
    grad_wv = jnp.dot(normed.T, value_gradient, preferred_element_type=jnp.float32).astype(jnp.bfloat16)
    back_terms = jnp.einsum('stc,dtc->tsd', convert_float(d_query).reshape(sequence_length, group_count, cols_q), convert_float(w_query).reshape(MODEL_WIDTH, group_count, cols_q))
    back_terms = back_terms + jnp.einsum('stc,dtc->tsd', convert_float(key_gradient).reshape(sequence_length, group_count, key_value_columns), convert_float(w_key).reshape(MODEL_WIDTH, group_count, key_value_columns))
    back_terms = back_terms + jnp.einsum('stc,dtc->tsd', convert_float(value_gradient).reshape(sequence_length, group_count, key_value_columns), convert_float(value_weight).reshape(MODEL_WIDTH, group_count, key_value_columns))
    d_normed = lax.optimization_barrier(jnp.sum(convert_float(back_terms.astype(jnp.bfloat16)), axis=0))
    gain_dn = d_normed * gain_vec
    grad_rows_f = convert_float(grad_rows)
    grad_input = (grad_rows_f + inv_rms * gain_dn - unit_rows * inv_rms * lax.optimization_barrier(jnp.mean(gain_dn * unit_rows, axis=1, keepdims=True))).astype(jnp.bfloat16)
    gain_term = lax.optimization_barrier(jnp.sum(d_normed * unit_rows, axis=0))
    return (layer_output, grad_input, gain_term, grad_wq, grad_wk, grad_wv, grad_wout)

def reference(layer_input, norm_gain, w_query, w_key, value_weight, w_out, prefix_len, grad_output):
    gain_vec = convert_float(norm_gain)
    outputs_list = []
    inputs_list = []
    gain_total = jnp.zeros((MODEL_WIDTH,), jnp.float32)
    sum_q = jnp.zeros(w_query.shape, jnp.float32)
    sum_k = jnp.zeros(w_key.shape, jnp.float32)
    sum_v = jnp.zeros(value_weight.shape, jnp.float32)
    sum_o = jnp.zeros(w_out.shape, jnp.float32)
    for replica_idx in range(N_DP):
        result = replica(layer_input[replica_idx], gain_vec, w_query, w_key, value_weight, w_out, prefix_len[replica_idx], grad_output[replica_idx])
        outputs_list.append(result[0])
        inputs_list.append(result[1])
        gain_total = gain_total + result[2]
        sum_q = sum_q + convert_float(result[3])
        sum_k = sum_k + convert_float(result[4])
        sum_v = sum_v + convert_float(result[5])
        sum_o = sum_o + convert_float(result[6])
    return (jnp.stack(outputs_list), jnp.stack(inputs_list), gain_total, sum_q.astype(jnp.bfloat16), sum_k.astype(jnp.bfloat16), sum_v.astype(jnp.bfloat16), sum_o.astype(jnp.bfloat16))
```

```python
import jax
import jax.numpy as jnp
from jax import lax
from jax.sharding import PartitionSpec as P

HEAD_SIZE = 128


EPS = 1e-05

NY = 4
NZ = 2


def convert_float(value):
    return value.astype(jnp.float32)


def _t(y, z):
    return (y % NY) * NZ + z


def _perm(fn):
    return [(t, fn(t)) for t in range(NY * NZ)]


YP = _perm(lambda t: _t(t // NZ + 1, t % NZ))
YM = _perm(lambda t: _t(t // NZ - 1, t % NZ))
ZZ = _perm(lambda t: t ^ 1)

SLOTS = ((0, 0), (-1, 0), (1, 0), (0, 1), (2, 0), (1, 1), (-1, 1), (2, 1))


def _pp(x, perm):
    return lax.ppermute(x, "tensor", perm)


def _thirds(cols):
    tiles = cols // 128
    a = (tiles + 2) // 3
    b = (tiles - a + 1) // 2
    return [(0, a * 128), (a * 128, (a + b) * 128), ((a + b) * 128, cols)]


def slot_tensor_index(me):
    y = me // NZ
    z = me % NZ
    return [_t(y + dy, z ^ dz) for dy, dz in SLOTS]


def gather_tensor(x):
    rows, cols = x.shape
    h = rows // 2
    a = _pp(x, YP)
    b = _pp(x, YM)
    c = _pp(x, ZZ)
    s_ym = _pp(jnp.concatenate([b[:h], c[:h]], 0), YM)
    s_yp = _pp(jnp.concatenate([a[h:], c[h:]], 0), YP)
    s_z = _pp(jnp.concatenate([b[h:], a[:h]], 0), ZZ)
    d = jnp.concatenate([s_ym[:h], s_yp[:h]], 0)
    e = jnp.concatenate([s_ym[h:], s_z[:h]], 0)
    f = jnp.concatenate([s_z[h:], s_yp[h:]], 0)
    (c0a, c0b), (c1a, c1b), (c2a, c2b) = _thirds(cols)
    g0 = _pp(d[:, c0a:c0b], ZZ)
    g1 = _pp(e[:, c1a:c1b], YM)
    g2 = _pp(f[:, c2a:c2b], YP)
    g = jnp.concatenate([g0, g1, g2], 1)
    return jnp.concatenate([x, a, b, c, d, e, f, g], 0)


def scatter_tensor(full, link_dtype):
    rows = full.shape[0] // len(SLOTS)
    cols = full.shape[1]
    h = rows // 2
    me, a, b, c, d, e, f, g = [full[i * rows:(i + 1) * rows] for i in range(len(SLOTS))]
    (c0a, c0b), (c1a, c1b), (c2a, c2b) = _thirds(cols)
    r_z = _pp(g[:, c0a:c0b].astype(link_dtype), ZZ)
    r_yp = _pp(g[:, c1a:c1b].astype(link_dtype), YP)
    r_ym = _pp(g[:, c2a:c2b].astype(link_dtype), YM)
    d = jnp.concatenate([d[:, :c0b] + convert_float(r_z), d[:, c0b:]], 1)
    e = jnp.concatenate([e[:, :c1a], e[:, c1a:c1b] + convert_float(r_yp), e[:, c1b:]], 1)
    f = jnp.concatenate([f[:, :c2a], f[:, c2a:] + convert_float(r_ym)], 1)
    s_yp = convert_float(_pp(jnp.concatenate([d[:h], e[:h]], 0).astype(link_dtype), YP))
    s_ym = convert_float(_pp(jnp.concatenate([d[h:], f[h:]], 0).astype(link_dtype), YM))
    s_z = convert_float(_pp(jnp.concatenate([e[h:], f[:h]], 0).astype(link_dtype), ZZ))
    b = b + jnp.concatenate([s_yp[:h], s_z[:h]], 0)
    c = c + jnp.concatenate([s_yp[h:], s_ym[h:]], 0)
    a = a + jnp.concatenate([s_z[h:], s_ym[:h]], 0)
    from_a = convert_float(_pp(a.astype(link_dtype), YM))
    from_b = convert_float(_pp(b.astype(link_dtype), YP))
    from_c = convert_float(_pp(c.astype(link_dtype), ZZ))
    return me + from_a + from_b + from_c


def per_device(
    layer_input, norm_gain, w_query, w_key, value_weight, w_out, prefix_len, grad_output
):
    heads_q = w_query.shape[1] // HEAD_SIZE
    heads_kv = w_key.shape[1] // HEAD_SIZE
    heads_per_group = heads_q // heads_kv
    scale_f = 1.0 / HEAD_SIZE**0.5
    rows_f = convert_float(layer_input[0])
    block_rows = rows_f.shape[0]
    gain_vec = convert_float(norm_gain)
    inv_rms = lax.rsqrt(jnp.mean(rows_f * rows_f, axis=1, keepdims=True) + EPS)
    unit_rows = rows_f * inv_rms
    normed = (unit_rows * gain_vec).astype(jnp.bfloat16)
    grad_local = grad_output[0]
    full_normed = gather_tensor(normed)
    full_grad = gather_tensor(grad_local)
    sequence_length = full_normed.shape[0]

    me = lax.axis_index("tensor")
    slot_t = jnp.stack(slot_tensor_index(me)).astype(jnp.int32)
    positions = (
        slot_t[:, None] * block_rows + lax.iota(jnp.int32, block_rows)[None, :]
    ).reshape(sequence_length)

    query_matrix = jnp.dot(full_normed, w_query, preferred_element_type=jnp.float32).astype(
        jnp.bfloat16
    )
    key_projected = jnp.dot(full_normed, w_key, preferred_element_type=jnp.float32).astype(
        jnp.bfloat16
    )
    value_projected = jnp.dot(full_normed, value_weight, preferred_element_type=jnp.float32).astype(
        jnp.bfloat16
    )
    query_head_rows = query_matrix.reshape(sequence_length, heads_kv, heads_per_group, HEAD_SIZE)
    key_head_rows = key_projected.reshape(sequence_length, heads_kv, HEAD_SIZE)
    value_head_rows = value_projected.reshape(sequence_length, heads_kv, HEAD_SIZE)
    allowed = (positions[None, :] <= positions[:, None]) | (positions[None, :] < prefix_len[0])
    scores = (
        jnp.einsum(
            "skgd,tkd->kgst", query_head_rows, key_head_rows, preferred_element_type=jnp.float32
        )
        * scale_f
    )
    masked = jnp.where(allowed, scores, -1e30)
    row_max = jnp.max(masked, axis=-1, keepdims=True)
    expo_vals = jnp.exp(masked - row_max)
    attn_probs = expo_vals / jnp.sum(expo_vals, axis=-1, keepdims=True)
    probability_batch = attn_probs.astype(jnp.bfloat16)
    context = (
        jnp.einsum(
            "kgst,tkd->skgd", probability_batch, value_head_rows, preferred_element_type=jnp.float32
        )
        .astype(jnp.bfloat16)
        .reshape(sequence_length, heads_q * HEAD_SIZE)
    )
    product = jnp.dot(context, w_out, preferred_element_type=jnp.float32)
    attn_sum = scatter_tensor(convert_float(product.astype(jnp.bfloat16)), jnp.bfloat16)
    layer_output = (rows_f + attn_sum).astype(jnp.bfloat16)[None]
    context_gradient = jnp.einsum(
        "sd,hd->sh", full_grad, w_out, preferred_element_type=jnp.float32
    ).astype(jnp.bfloat16)
    wout_term = jnp.einsum(
        "sh,sd->hd", context, full_grad, preferred_element_type=jnp.float32
    ).astype(jnp.bfloat16)
    context_head_gradient = context_gradient.reshape(
        sequence_length, heads_kv, heads_per_group, HEAD_SIZE
    )
    d_probs = jnp.einsum(
        "skgd,tkd->kgst", context_head_gradient, value_head_rows, preferred_element_type=jnp.float32
    )
    row_delta = jnp.sum(d_probs * attn_probs, axis=-1, keepdims=True)
    scores_gradient = (attn_probs * (d_probs - row_delta) * scale_f).astype(jnp.bfloat16)
    d_query = (
        jnp.einsum(
            "kgst,tkd->skgd", scores_gradient, key_head_rows, preferred_element_type=jnp.float32
        )
        .astype(jnp.bfloat16)
        .reshape(sequence_length, heads_q * HEAD_SIZE)
    )
    key_gradient = (
        jnp.einsum(
            "apyq,yapz->qaz", scores_gradient, query_head_rows, preferred_element_type=jnp.float32
        )
        .astype(jnp.bfloat16)
        .reshape(sequence_length, heads_kv * HEAD_SIZE)
    )
    value_gradient = (
        jnp.einsum(
            "apyq,yapz->qaz",
            probability_batch,
            context_head_gradient,
            preferred_element_type=jnp.float32,
        )
        .astype(jnp.bfloat16)
        .reshape(sequence_length, heads_kv * HEAD_SIZE)
    )
    summed = jnp.einsum("sh,dh->sd", d_query, w_query, preferred_element_type=jnp.float32)
    summed = summed + jnp.einsum(
        "sh,dh->sd", key_gradient, w_key, preferred_element_type=jnp.float32
    )
    summed = summed + jnp.einsum(
        "sh,dh->sd", value_gradient, value_weight, preferred_element_type=jnp.float32
    )
    d_normed = scatter_tensor(convert_float(summed.astype(jnp.bfloat16)), jnp.bfloat16)
    gain_dn = d_normed * gain_vec
    grad_input = (
        convert_float(grad_local)
        + inv_rms * gain_dn
        - unit_rows * inv_rms * jnp.mean(gain_dn * unit_rows, axis=1, keepdims=True)
    ).astype(jnp.bfloat16)[None]
    gain_term = jnp.sum(d_normed * unit_rows, axis=0)
    query_term = jnp.einsum(
        "sd,sh->dh", full_normed, d_query, preferred_element_type=jnp.float32
    ).astype(jnp.bfloat16)
    key_term = jnp.einsum(
        "sd,sh->dh", full_normed, key_gradient, preferred_element_type=jnp.float32
    ).astype(jnp.bfloat16)
    value_term = jnp.einsum(
        "sd,sh->dh", full_normed, value_gradient, preferred_element_type=jnp.float32
    ).astype(jnp.bfloat16)
    n_dp = lax.psum(1, "dp")
    width = query_term.shape[0]
    out_rows = w_out.shape[0]
    wq_cols = query_term.shape[1]
    wk_cols = key_term.shape[1]
    wv_cols = value_term.shape[1]
    wo_cols = width // n_dp
    wout_blocks = wout_term.reshape(out_rows, n_dp, wo_cols).transpose(1, 0, 2)
    packed = jnp.concatenate(
        [
            query_term.reshape(n_dp, width // n_dp, wq_cols),
            key_term.reshape(n_dp, width // n_dp, wk_cols),
            value_term.reshape(n_dp, width // n_dp, wv_cols),
            wout_blocks,
        ],
        axis=2,
    )
    reduced = lax.psum_scatter(packed, "dp", scatter_dimension=0, tiled=True)[0]
    sum_q = reduced[:, :wq_cols]
    sum_k = reduced[:, wq_cols:wq_cols + wk_cols]
    sum_v = reduced[:, wq_cols + wk_cols:wq_cols + wk_cols + wv_cols]
    grad_wout = reduced[:, wq_cols + wk_cols + wv_cols:]
    grad_gain = lax.psum(gain_term, ("dp", "tensor"))
    return (
        layer_output,
        grad_input,
        grad_gain,
        sum_q,
        sum_k,
        sum_v,
        grad_wout,
    )


def solution(mesh):
    in_specs = (
        P("dp", "tensor", None),
        P(),
        P(None, "tensor"),
        P(None, "tensor"),
        P(None, "tensor"),
        P("tensor", None),
        P("dp"),
        P("dp", "tensor", None),
    )
    out_specs = (
        P("dp", "tensor", None),
        P("dp", "tensor", None),
        P(),
        P("dp", "tensor"),
        P("dp", "tensor"),
        P("dp", "tensor"),
        P("tensor", "dp"),
    )
    return jax.shard_map(
        per_device, mesh=mesh, in_specs=in_specs, out_specs=out_specs, check_vma=False
    )
```

```python
import jax
import jax.numpy as jnp
from jax import lax
from jax.sharding import PartitionSpec as P

HEAD_SIZE = 128


EPS = 1e-05

NY = 4
NZ = 2


def convert_float(value):
    return value.astype(jnp.float32)


def _t(y, z):
    return (y % NY) * NZ + z


def _perm(fn):
    return [(t, fn(t)) for t in range(NY * NZ)]


YP = _perm(lambda t: _t(t // NZ + 1, t % NZ))
YM = _perm(lambda t: _t(t // NZ - 1, t % NZ))
ZZ = _perm(lambda t: t ^ 1)

SLOTS = ((0, 0), (-1, 0), (1, 0), (0, 1), (2, 0), (1, 1), (-1, 1), (2, 1))


def _pp(x, perm):
    return lax.ppermute(x, "tensor", perm)


def _thirds(cols):
    tiles = cols // 128
    a = (tiles + 2) // 3
    b = (tiles - a + 1) // 2
    return [(0, a * 128), (a * 128, (a + b) * 128), ((a + b) * 128, cols)]


def slot_tensor_index(me):
    y = me // NZ
    z = me % NZ
    return [_t(y + dy, z ^ dz) for dy, dz in SLOTS]


def gather_tensor(x):
    rows, cols = x.shape
    h = rows // 2
    a = _pp(x, YP)
    b = _pp(x, YM)
    c = _pp(x, ZZ)
    s_ym = _pp(jnp.concatenate([b[:h], c[:h]], 0), YM)
    s_yp = _pp(jnp.concatenate([a[h:], c[h:]], 0), YP)
    s_z = _pp(jnp.concatenate([b[h:], a[:h]], 0), ZZ)
    d = jnp.concatenate([s_ym[:h], s_yp[:h]], 0)
    e = jnp.concatenate([s_ym[h:], s_z[:h]], 0)
    f = jnp.concatenate([s_z[h:], s_yp[h:]], 0)
    (c0a, c0b), (c1a, c1b), (c2a, c2b) = _thirds(cols)
    g0 = _pp(d[:, c0a:c0b], ZZ)
    g1 = _pp(e[:, c1a:c1b], YM)
    g2 = _pp(f[:, c2a:c2b], YP)
    g = jnp.concatenate([g0, g1, g2], 1)
    return jnp.concatenate([x, a, b, c, d, e, f, g], 0)


def scatter_tensor(full, link_dtype):
    rows = full.shape[0] // len(SLOTS)
    cols = full.shape[1]
    h = rows // 2
    me, a, b, c, d, e, f, g = [full[i * rows:(i + 1) * rows] for i in range(len(SLOTS))]
    (c0a, c0b), (c1a, c1b), (c2a, c2b) = _thirds(cols)
    r_z = _pp(g[:, c0a:c0b].astype(link_dtype), ZZ)
    r_yp = _pp(g[:, c1a:c1b].astype(link_dtype), YP)
    r_ym = _pp(g[:, c2a:c2b].astype(link_dtype), YM)
    d = jnp.concatenate([d[:, :c0b] + convert_float(r_z), d[:, c0b:]], 1)
    e = jnp.concatenate([e[:, :c1a], e[:, c1a:c1b] + convert_float(r_yp), e[:, c1b:]], 1)
    f = jnp.concatenate([f[:, :c2a], f[:, c2a:] + convert_float(r_ym)], 1)
    s_yp = convert_float(_pp(jnp.concatenate([d[:h], e[:h]], 0).astype(link_dtype), YP))
    s_ym = convert_float(_pp(jnp.concatenate([d[h:], f[h:]], 0).astype(link_dtype), YM))
    s_z = convert_float(_pp(jnp.concatenate([e[h:], f[:h]], 0).astype(link_dtype), ZZ))
    b = b + jnp.concatenate([s_yp[:h], s_z[:h]], 0)
    c = c + jnp.concatenate([s_yp[h:], s_ym[h:]], 0)
    a = a + jnp.concatenate([s_z[h:], s_ym[:h]], 0)
    from_a = convert_float(_pp(a.astype(link_dtype), YM))
    from_b = convert_float(_pp(b.astype(link_dtype), YP))
    from_c = convert_float(_pp(c.astype(link_dtype), ZZ))
    return me + from_a + from_b + from_c


def _dp_perm(fn):
    return [(d, fn(d)) for d in range(DP_SIZE)]


DP_SIZE = 16
DP_XOR = (1, 2, 4, 8)
T_XOR = (1, 2, 4)


def butterfly_sum(v):
    for k in DP_XOR:
        v = v + lax.ppermute(v, "dp", _dp_perm(lambda d, k=k: d ^ k))
    for k in T_XOR:
        v = v + _pp(v, _perm(lambda t, k=k: t ^ k))
    return v


def per_device(
    layer_input, norm_gain, w_query, w_key, value_weight, w_out, prefix_len, grad_output
):
    heads_q = w_query.shape[1] // HEAD_SIZE
    heads_kv = w_key.shape[1] // HEAD_SIZE
    heads_per_group = heads_q // heads_kv
    scale_f = 1.0 / HEAD_SIZE**0.5
    rows_f = convert_float(layer_input[0])
    block_rows = rows_f.shape[0]
    gain_vec = convert_float(norm_gain)
    inv_rms = lax.rsqrt(jnp.mean(rows_f * rows_f, axis=1, keepdims=True) + EPS)
    unit_rows = rows_f * inv_rms
    normed = (unit_rows * gain_vec).astype(jnp.bfloat16)
    full_normed = gather_tensor(normed)
    full_normed, grad_local = lax.optimization_barrier((full_normed, grad_output[0]))
    full_grad = gather_tensor(grad_local)
    sequence_length = full_normed.shape[0]

    me = lax.axis_index("tensor")
    slot_t = jnp.stack(slot_tensor_index(me)).astype(jnp.int32)
    positions = (
        slot_t[:, None] * block_rows + lax.iota(jnp.int32, block_rows)[None, :]
    ).reshape(sequence_length)

    query_matrix = jnp.dot(full_normed, w_query, preferred_element_type=jnp.float32).astype(
        jnp.bfloat16
    )
    key_projected = jnp.dot(full_normed, w_key, preferred_element_type=jnp.float32).astype(
        jnp.bfloat16
    )
    value_projected = jnp.dot(full_normed, value_weight, preferred_element_type=jnp.float32).astype(
        jnp.bfloat16
    )
    query_head_rows = query_matrix.reshape(sequence_length, heads_kv, heads_per_group, HEAD_SIZE)
    key_head_rows = key_projected.reshape(sequence_length, heads_kv, HEAD_SIZE)
    value_head_rows = value_projected.reshape(sequence_length, heads_kv, HEAD_SIZE)
    allowed = (positions[None, :] <= positions[:, None]) | (positions[None, :] < prefix_len[0])
    scores = (
        jnp.einsum(
            "skgd,tkd->kgst", query_head_rows, key_head_rows, preferred_element_type=jnp.float32
        )
        * scale_f
    )
    masked = jnp.where(allowed, scores, -1e30)
    row_max = jnp.max(masked, axis=-1, keepdims=True)
    expo_vals = jnp.exp(masked - row_max)
    attn_probs = expo_vals / jnp.sum(expo_vals, axis=-1, keepdims=True)
    probability_batch = attn_probs.astype(jnp.bfloat16)
    context = (
        jnp.einsum(
            "kgst,tkd->skgd", probability_batch, value_head_rows, preferred_element_type=jnp.float32
        )
        .astype(jnp.bfloat16)
        .reshape(sequence_length, heads_q * HEAD_SIZE)
    )
    product = jnp.dot(context, w_out, preferred_element_type=jnp.float32)
    attn_sum = scatter_tensor(convert_float(product.astype(jnp.bfloat16)), jnp.bfloat16)
    layer_output = (rows_f + attn_sum).astype(jnp.bfloat16)[None]
    context_gradient = jnp.einsum(
        "sd,hd->sh", full_grad, w_out, preferred_element_type=jnp.float32
    ).astype(jnp.bfloat16)
    wout_term = jnp.einsum(
        "sh,sd->hd", context, full_grad, preferred_element_type=jnp.float32
    ).astype(jnp.bfloat16)
    context_head_gradient = context_gradient.reshape(
        sequence_length, heads_kv, heads_per_group, HEAD_SIZE
    )
    d_probs = jnp.einsum(
        "skgd,tkd->kgst", context_head_gradient, value_head_rows, preferred_element_type=jnp.float32
    )
    row_delta = jnp.sum(d_probs * attn_probs, axis=-1, keepdims=True)
    scores_gradient = (attn_probs * (d_probs - row_delta) * scale_f).astype(jnp.bfloat16)
    d_query = (
        jnp.einsum(
            "kgst,tkd->skgd", scores_gradient, key_head_rows, preferred_element_type=jnp.float32
        )
        .astype(jnp.bfloat16)
        .reshape(sequence_length, heads_q * HEAD_SIZE)
    )
    key_gradient = (
        jnp.einsum(
            "apyq,yapz->qaz", scores_gradient, query_head_rows, preferred_element_type=jnp.float32
        )
        .astype(jnp.bfloat16)
        .reshape(sequence_length, heads_kv * HEAD_SIZE)
    )
    value_gradient = (
        jnp.einsum(
            "apyq,yapz->qaz",
            probability_batch,
            context_head_gradient,
            preferred_element_type=jnp.float32,
        )
        .astype(jnp.bfloat16)
        .reshape(sequence_length, heads_kv * HEAD_SIZE)
    )
    summed = jnp.einsum("sh,dh->sd", d_query, w_query, preferred_element_type=jnp.float32)
    summed = summed + jnp.einsum(
        "sh,dh->sd", key_gradient, w_key, preferred_element_type=jnp.float32
    )
    summed = summed + jnp.einsum(
        "sh,dh->sd", value_gradient, value_weight, preferred_element_type=jnp.float32
    )
    d_normed = scatter_tensor(convert_float(summed.astype(jnp.bfloat16)), jnp.bfloat16)
    gain_dn = d_normed * gain_vec
    grad_input = (
        convert_float(grad_local)
        + inv_rms * gain_dn
        - unit_rows * inv_rms * jnp.mean(gain_dn * unit_rows, axis=1, keepdims=True)
    ).astype(jnp.bfloat16)[None]
    gain_term = jnp.sum(d_normed * unit_rows, axis=0)
    query_term = jnp.einsum(
        "sd,sh->dh", full_normed, d_query, preferred_element_type=jnp.float32
    ).astype(jnp.bfloat16)
    key_term = jnp.einsum(
        "sd,sh->dh", full_normed, key_gradient, preferred_element_type=jnp.float32
    ).astype(jnp.bfloat16)
    value_term = jnp.einsum(
        "sd,sh->dh", full_normed, value_gradient, preferred_element_type=jnp.float32
    ).astype(jnp.bfloat16)
    n_dp = lax.psum(1, "dp")
    width = query_term.shape[0]
    out_rows = w_out.shape[0]
    wq_cols = query_term.shape[1]
    wk_cols = key_term.shape[1]
    wv_cols = value_term.shape[1]
    wo_cols = width // n_dp
    wout_blocks = wout_term.reshape(out_rows, n_dp, wo_cols).transpose(1, 0, 2)
    packed = jnp.concatenate(
        [
            query_term.reshape(n_dp, width // n_dp, wq_cols),
            key_term.reshape(n_dp, width // n_dp, wk_cols),
            value_term.reshape(n_dp, width // n_dp, wv_cols),
            wout_blocks,
        ],
        axis=2,
    )
    reduced = lax.psum_scatter(packed, "dp", scatter_dimension=0, tiled=True)[0]
    sum_q = reduced[:, :wq_cols]
    sum_k = reduced[:, wq_cols:wq_cols + wk_cols]
    sum_v = reduced[:, wq_cols + wk_cols:wq_cols + wk_cols + wv_cols]
    grad_wout = reduced[:, wq_cols + wk_cols + wv_cols:]
    grad_gain = butterfly_sum(gain_term)
    return (
        layer_output,
        grad_input,
        grad_gain,
        sum_q,
        sum_k,
        sum_v,
        grad_wout,
    )


def solution(mesh):
    in_specs = (
        P("dp", "tensor", None),
        P(),
        P(None, "tensor"),
        P(None, "tensor"),
        P(None, "tensor"),
        P("tensor", None),
        P("dp"),
        P("dp", "tensor", None),
    )
    out_specs = (
        P("dp", "tensor", None),
        P("dp", "tensor", None),
        P(),
        P("dp", "tensor"),
        P("dp", "tensor"),
        P("dp", "tensor"),
        P("tensor", "dp"),
    )
    return jax.shard_map(
        per_device, mesh=mesh, in_specs=in_specs, out_specs=out_specs, check_vma=False
    )
```
